512 devices in a mesh: dp: 16 (over z, core), expert: 32 (over x, y).
Axes of the slice: x: 4, y: 8, z: 8, core: 2. Of those that a mesh axis runs over, the one named last changes fastest.
Arguments:
- out_grad: bfloat16 [65536, 1024], P(('dp', 'expert')), may hold values from -6 to 6
- hidden: bfloat16 [65536, 8, 384], P(('dp', 'expert')), may hold values from -1.5 to 1.5
- gate: bfloat16 [65536, 8], P(('dp', 'expert')), may hold values from 0.049804688 to 0.5
- route_expert: int32 [65536, 8], P(('dp', 'expert')), may hold values from 0 to 63, as said below
- route_replica: int32 [65536, 8], P(('dp', 'expert')), may hold values from 0 to 3, as said below
- slot_expert: int32 [32, 3], replicated, may hold values from 0 to 63, as said below
- down_weight: bfloat16 [32, 3, 384, 1024], P('expert')
Outputs:
- d_hidden: bfloat16 [65536, 8, 384], P(('dp', 'expert'))
- d_gate: bfloat16 [65536, 8], P(('dp', 'expert'))
- d_weight: float32 [32, 3, 384, 1024], P('expert', None, 'dp')
The draws below stay inside these ranges and needn't reach their ends.
Inputs may be any that keep to these rules, and one draw needn't show every extreme that they name: `slot_expert`: every expert holds 1 to 4 slots: exactly 8 experts hold 4, 8 hold 2, the rest 1. `route_expert`: the 8 experts of a token differ. Of the routes of one device's 128 tokens, at most 16 go to one slot, and some slot receives exactly 16 routes from every device. route_replica is below the number of slots of the route's expert.
All inputs are finite; a program needn't handle non-finite values.
Results may differ from the reference program's by a relative error of at most 0.0029.
Values may be sent and summed in bfloat16 or wider, within the bound.
No kernel may reach another device: no remote copies, remote signals or barrier semaphores. Data moves between devices by JAX's collectives and lax.ppermute only.
A program may use at most 128 MiB of HBM per device.

```python
import math
import jax
import jax.numpy as jnp
from jax import lax

D = 1024
F = 384
EXPERTS = 64
K = 8
TOK_DEV = 128
SLOTS = 3
CAP = 16
TOKENS = 65536
N_DP = 16
N_EXPERT = 32


def layout(key):
    base_key = jax.random.fold_in(key, 7)
    subkeys = jax.random.split(base_key, 8)
    slot_count = 3 * EXPERTS // 2
    expert_rank = jnp.arange(EXPERTS, dtype=jnp.int32)
    copies = jnp.where(expert_rank < EXPERTS // 8, 4, jnp.where(expert_rank < EXPERTS // 4, 2, 1)).astype(jnp.int32)
    run_ends = jnp.cumsum(copies)
    canonical = jnp.arange(slot_count, dtype=jnp.int32)
    rank_of = jnp.sum((run_ends[None, :] <= canonical[:, None]).astype(jnp.int32), axis=1)
    ordering = jax.random.permutation(subkeys[0], EXPERTS).astype(jnp.int32)
    expert_of = ordering[rank_of]
    placement = jax.random.permutation(subkeys[1], slot_count).astype(jnp.int32)
    flat_slots = jnp.zeros((slot_count,), jnp.int32).at[placement].set(expert_of)
    same_expert = expert_of[:, None] == expert_of[None, :]
    replica_of = jnp.sum((same_expert & (placement[None, :] < placement[:, None])).astype(jnp.int32), axis=1)
    return (flat_slots, expert_of, replica_of, subkeys)


def routing(key):
    flat_slots, expert_of, replica_of, subkeys = layout(key)
    slot_count = expert_of.shape[0]
    hot_slots = 3 * EXPERTS // 4
    cold_slots = slot_count - hot_slots
    blocks = N_DP * N_EXPERT
    routes = TOK_DEV * K
    hot_counts = jax.random.randint(subkeys[2], (blocks, hot_slots), CAP // 2, CAP + 1)
    everywhere = jax.random.randint(subkeys[3], (), 0, hot_slots)
    per_block = jax.random.randint(subkeys[4], (blocks,), 0, hot_slots)
    column = jnp.arange(hot_slots)[None, :]
    hot_counts = jnp.where((column == everywhere) | (column == per_block[:, None]), CAP, hot_counts)
    remaining = routes - jnp.sum(hot_counts, axis=1)
    base_count = remaining // cold_slots
    extra_count = remaining % cold_slots
    cold_order = jax.vmap(lambda subkey: jax.random.permutation(subkey, cold_slots))(jax.random.split(subkeys[5], blocks))
    cold_counts = base_count[:, None] + (cold_order < extra_count[:, None]).astype(jnp.int32)
    counts = jnp.concatenate([hot_counts, cold_counts], axis=1).astype(jnp.int32)
    run_ends = jnp.cumsum(counts, axis=1)
    route_index = jnp.arange(routes, dtype=jnp.int32)

    def canon_block(block_ends):
        return jnp.sum((block_ends[None, :] <= route_index[:, None]).astype(jnp.int32), axis=1)
    canonical = lax.map(canon_block, run_ends)
    experts = jnp.swapaxes(expert_of[canonical].reshape(blocks, K, TOK_DEV), 1, 2)
    replicas = jnp.swapaxes(replica_of[canonical].reshape(blocks, K, TOK_DEV), 1, 2)
    token_order = jax.vmap(lambda subkey: jax.random.permutation(subkey, TOK_DEV))(jax.random.split(subkeys[6], blocks))
    experts = jnp.take_along_axis(experts, token_order[:, :, None], axis=1)
    replicas = jnp.take_along_axis(replicas, token_order[:, :, None], axis=1)
    scores = jax.random.randint(subkeys[7], (blocks, TOK_DEV, K), 0, 1 << 20) * K + jnp.arange(K, dtype=jnp.int32)
    column_order = jnp.argsort(scores, axis=2).astype(jnp.int32)
    experts = jnp.take_along_axis(experts, column_order, axis=2)
    replicas = jnp.take_along_axis(replicas, column_order, axis=2)
    return (experts.reshape(TOKENS, K).astype(jnp.int32), replicas.reshape(TOKENS, K).astype(jnp.int32))


def draw_route_expert(key, part):
    return routing(key)[0]


def draw_route_replica(key, part):
    return routing(key)[1]


def draw_slot_expert(key, part):
    return layout(key)[0].reshape(N_EXPERT, SLOTS)


def draw_down_weight(key, part):
    flat_slots = layout(key)[0]
    weight_key = jax.random.fold_in(key, 11)

    def one_expert(expert):
        subkey = jax.random.fold_in(weight_key, expert)
        values = jax.random.normal(subkey, (F, D), jnp.float32)
        return values * F ** (-0.5)
    stacked = jax.vmap(one_expert)(flat_slots)
    return stacked.reshape(N_EXPERT, SLOTS, F, D).astype(jnp.bfloat16)


def level_of(own_key, extent, cuts, least, top_value):
    def one(dim, blocks):
        heights = jax.random.uniform(jax.random.fold_in(jax.random.fold_in(own_key, 6), dim), (blocks,), jnp.float32, least / len(cuts), top_value / len(cuts))
        return jnp.repeat(jnp.exp(heights), extent[dim] // blocks).reshape((-1,) + (1,) * (len(extent) - dim - 1))

    level = one(*cuts[0])
    for cut in cuts[1:]:
        level = level * one(*cut)
    return level


def bell_draw(rng, extent, scale, limit, shards=(), held_as=jnp.bfloat16):
    gain = level_of(rng, extent, shards, -0.22, 0.18) if shards else 1.0
    values = jax.random.normal(rng, extent, jnp.float32) * scale * gain
    return jnp.minimum(jnp.maximum(values, -limit), limit).astype(held_as)


def setup_inputs(seed: int = 0) -> dict:
    key_of = jax.random.split(jax.random.key(seed), 8)
    out_grad = bell_draw(key_of[0], (TOKENS, D), 1.0, 6.0, ((0, 512),))
    hidden = bell_draw(key_of[1], (TOKENS, K, F), 0.25, 1.5, ((0, 512),))
    gate = jnp.clip(jnp.exp(math.log(0.5) - 2.306499 * jax.random.uniform(key_of[2], (TOKENS, K), jnp.float32) ** level_of(key_of[2], (TOKENS, K), ((0, 512),), -0.2, 0.2)), 0.049804688, 0.5).astype(jnp.bfloat16)
    route_expert = draw_route_expert(jax.random.fold_in(key_of[7], 71), 0)
    route_replica = draw_route_replica(jax.random.fold_in(key_of[7], 71), 0)
    slot_expert = draw_slot_expert(jax.random.fold_in(key_of[7], 71), 0)
    down_weight = draw_down_weight(jax.random.fold_in(key_of[7], 71), 0)
    return {"out_grad": out_grad, "hidden": hidden, "gate": gate, "route_expert": route_expert, "route_replica": route_replica, "slot_expert": slot_expert, "down_weight": down_weight}


def slot_lookup(flat_slots):
    slot_count = flat_slots.shape[0]
    ordering = jnp.arange(slot_count, dtype=jnp.int32)
    same_expert = flat_slots[:, None] == flat_slots[None, :]
    replica_rank = jnp.sum((same_expert & (ordering[None, :] < ordering[:, None])).astype(jnp.int32), axis=1)
    expert_ids = jnp.arange(EXPERTS, dtype=jnp.int32)
    replica_ids = jnp.arange(4, dtype=jnp.int32)
    matches = (flat_slots[None, None, :] == expert_ids[:, None, None]) & (replica_rank[None, None, :] == replica_ids[None, :, None])
    return jnp.sum(jnp.where(matches, ordering[None, None, :], 0), axis=2).astype(jnp.int32)


def reference(out_grad, hidden, gate, route_expert, route_replica, slot_expert, down_weight):
    flat_slots = slot_expert.reshape(-1)
    slot_count = flat_slots.shape[0]
    route_count = TOKENS * K
    group_rows = N_EXPERT * CAP
    destination = slot_lookup(flat_slots)[route_expert, route_replica].reshape(-1)
    route_group = (jnp.arange(route_count, dtype=jnp.int32) // K) // (TOK_DEV * N_EXPERT)
    sort_key = destination * N_DP + route_group
    sorted_routes = jnp.argsort(sort_key, stable=True).astype(jnp.int32)
    group_sizes = jax.ops.segment_sum(jnp.ones((route_count,), jnp.int32), sort_key, num_segments=slot_count * N_DP)
    group_starts = (jnp.cumsum(group_sizes) - group_sizes).astype(jnp.int32)
    hidden_flat = hidden.reshape(route_count, F)
    gate_flat = gate.reshape(route_count)
    weight_flat = down_weight.reshape(slot_count, F, D)
    offsets = jnp.arange(group_rows, dtype=jnp.int32)

    def per_slot(slot_index):
        begins = lax.dynamic_slice_in_dim(group_starts, slot_index * N_DP, N_DP)
        filled = lax.dynamic_slice_in_dim(group_sizes, slot_index * N_DP, N_DP)
        present = offsets[None, :] < filled[:, None]
        spots = jnp.minimum(begins[:, None] + offsets[None, :], route_count - 1)
        route_ids = jnp.where(present, sorted_routes[spots], 0)
        weight_mask = present.astype(jnp.float32)
        grad_rows = out_grad[route_ids // K].astype(jnp.float32) * weight_mask[..., None]
        hid_rows = hidden_flat[route_ids].astype(jnp.float32) * weight_mask[..., None]
        gate_rows = gate_flat[route_ids].astype(jnp.float32) * weight_mask
        weight = lax.dynamic_index_in_dim(weight_flat, slot_index, 0, keepdims=False).astype(jnp.float32)
        projected = jnp.einsum("pcd,fd->pcf", grad_rows, weight)
        row_grads = (gate_rows[..., None] * projected).astype(jnp.bfloat16)
        gate_grads = jnp.sum(hid_rows * projected, axis=-1).astype(jnp.bfloat16)
        scaled = lax.optimization_barrier((gate_rows[..., None] * hid_rows).astype(jnp.bfloat16)).astype(jnp.float32)
        partial_value = jnp.einsum("pcf,pcd->pfd", scaled, grad_rows)
        target = jnp.where(present, route_ids, route_count)
        return jnp.sum(partial_value, axis=0), row_grads, gate_grads, target

    group_sum, row_grads, gate_grads, targets = lax.map(per_slot, jnp.arange(slot_count, dtype=jnp.int32))
    flat_targets = targets.reshape(-1)
    d_hidden = jnp.zeros((route_count + 1, F), jnp.bfloat16).at[flat_targets].set(row_grads.reshape(-1, F))[:route_count]
    d_gate = jnp.zeros((route_count + 1,), jnp.bfloat16).at[flat_targets].set(gate_grads.reshape(-1))[:route_count]
    same_expert = (flat_slots[:, None] == flat_slots[None, :]).astype(jnp.float32)
    d_weight = jnp.einsum("st,tfd->sfd", same_expert, group_sum, precision=lax.Precision.HIGHEST)
    return (d_hidden.reshape(TOKENS, K, F), d_gate.reshape(TOKENS, K), d_weight.reshape(N_EXPERT, SLOTS, F, D))
```

```python
import jax
import jax.numpy as jnp
from jax import lax
from jax.sharding import PartitionSpec as P

EXPERTS = 64
CAP = 16
HOT = 16


def slot_of_route(experts, replicas, flat_slots):
    slot_count = flat_slots.shape[0]
    ordering = jnp.arange(slot_count, dtype=jnp.int32)
    same_expert = flat_slots[:, None] == flat_slots[None, :]
    replica_rank = jnp.sum(
        (same_expert & (ordering[None, :] < ordering[:, None])).astype(jnp.int32), axis=1
    )
    matches = (experts.reshape(-1)[:, None] == flat_slots[None, :]) & (
        replicas.reshape(-1)[:, None] == replica_rank[None, :]
    )
    return jnp.sum(jnp.where(matches, ordering[None, :], 0), axis=1)


def buffer_places(experts, replicas, flat_slots, capacity):
    destination = slot_of_route(experts, replicas, flat_slots)
    slot_count = flat_slots.shape[0]
    route_count = destination.shape[0]
    ordering = jnp.arange(route_count, dtype=jnp.int32)
    earlier = (destination[:, None] == destination[None, :]) & (ordering[None, :] < ordering[:, None])
    position = jnp.sum(earlier.astype(jnp.int32), axis=1)
    return destination * capacity + position


def route_of_place(places, length):
    route_count = places.shape[0]
    return (
        jnp.full((length,), route_count, jnp.int32)
        .at[places]
        .set(jnp.arange(route_count, dtype=jnp.int32))
    )


def exchange_sum(x, axis, count):
    pieces = lax.all_to_all(x.reshape(count, -1), axis, split_axis=0, concat_axis=0, tiled=True)
    own_total = jnp.sum(pieces, axis=0)
    copies = jnp.broadcast_to(own_total[None], pieces.shape)
    totals = lax.all_to_all(copies, axis, split_axis=0, concat_axis=0, tiled=True)
    return totals.reshape(x.shape)


def per_device(out_grad, hidden, gate, route_expert, route_replica, slot_expert, down_weight):
    tok_rows, chosen_count = gate.shape
    model_width = out_grad.shape[1]
    hidden_width = hidden.shape[2]
    groups, slots = slot_expert.shape
    flat_slots = slot_expert.reshape(-1)
    capacity = CAP
    block_rows = slots * capacity
    length = groups * block_rows
    route_count = tok_rows * chosen_count
    own_index = lax.axis_index("expert")
    places = buffer_places(route_expert, route_replica, flat_slots, capacity)
    source_route = route_of_place(places, length)
    hidden_rows = jnp.concatenate(
        [hidden.reshape(route_count, hidden_width), jnp.zeros((1, hidden_width), hidden.dtype)],
        axis=0,
    )
    gate_rows = jnp.concatenate([gate.reshape(route_count), jnp.zeros((1,), gate.dtype)])
    sent_hidden = hidden_rows[source_route].reshape(groups, block_rows, hidden_width)
    sent_gate = gate_rows[source_route].reshape(groups, block_rows)
    padded_grad = jnp.concatenate([out_grad, jnp.zeros((1, model_width), out_grad.dtype)], axis=0)
    token_rows = jnp.where(source_route < route_count, source_route // chosen_count, tok_rows)
    sent_grad = padded_grad[token_rows].reshape(groups, block_rows, model_width)
    got_grad, got_hidden, got_gate = (
        lax.all_to_all(sent_grad, "expert", split_axis=0, concat_axis=0, tiled=True),
        lax.all_to_all(sent_hidden, "expert", split_axis=0, concat_axis=0, tiled=True),
        lax.all_to_all(sent_gate, "expert", split_axis=0, concat_axis=0, tiled=True),
    )
    weights = down_weight[0]
    grad_four = got_grad.reshape(groups, slots, capacity, model_width)
    hidden_four = got_hidden.reshape(groups, slots, capacity, hidden_width)
    gate_four = got_gate.reshape(groups, slots, capacity).astype(jnp.float32)[..., None]
    projected = jnp.einsum("xscd,sfd->xscf", grad_four, weights, preferred_element_type=jnp.float32)
    back_rows = (
        (gate_four * projected).astype(jnp.bfloat16).reshape(groups, block_rows, hidden_width)
    )
    back_gate = (
        jnp.sum(hidden_four.astype(jnp.float32) * projected, axis=-1)
        .astype(jnp.bfloat16)
        .reshape(groups, block_rows)
    )
    came_rows, came_gate = (
        lax.all_to_all(back_rows, "expert", split_axis=0, concat_axis=0, tiled=True),
        lax.all_to_all(back_gate, "expert", split_axis=0, concat_axis=0, tiled=True),
    )
    d_hidden = came_rows.reshape(length, hidden_width)[places].reshape(
        tok_rows, chosen_count, hidden_width
    )
    d_gate = came_gate.reshape(length)[places].reshape(tok_rows, chosen_count)
    scaled = (gate_four * hidden_four.astype(jnp.float32)).astype(jnp.bfloat16)
    partial_value = jnp.einsum(
        "xscf,xscd->sfd", scaled, grad_four, preferred_element_type=jnp.float32
    )
    group_sum = lax.psum_scatter(partial_value, "dp", scatter_dimension=1, tiled=True)
    own_slots = lax.dynamic_slice_in_dim(flat_slots, own_index * slots, slots)
    expert_ids = jnp.arange(EXPERTS, dtype=jnp.int32)
    copies = jnp.sum((flat_slots[:, None] == expert_ids[None, :]).astype(jnp.int32), axis=0)
    is_hot = copies >= 2
    hot_rank = jnp.cumsum(is_hot.astype(jnp.int32)) - 1
    picks = own_slots[:, None] == expert_ids[None, :]
    slot_hot = jnp.any(picks & is_hot[None, :], axis=1)
    slot_rank = jnp.sum(jnp.where(picks, hot_rank[None, :], 0), axis=1)
    member = (slot_rank[:, None] == jnp.arange(HOT, dtype=jnp.int32)[None, :]) & slot_hot[:, None]
    hot_table = jnp.sum(jnp.where(member[:, :, None, None], group_sum[:, None], 0.0), axis=0)
    hot_total = exchange_sum(hot_table, "expert", lax.axis_size("expert"))
    from_table = jnp.sum(jnp.where(member[:, :, None, None], hot_total[None], 0.0), axis=1)
    d_weight = jnp.where(slot_hot[:, None, None], from_table, group_sum)[None]
    return (d_hidden, d_gate, d_weight)


def solution(mesh):
    placed = (
        P(("dp", "expert"), None),
        P(("dp", "expert"), None, None),
        P(("dp", "expert"), None),
        P(("dp", "expert"), None),
        P(("dp", "expert"), None),
        P(),
        P("expert", None, None, None),
    )
    return jax.shard_map(
        per_device,
        mesh=mesh,
        in_specs=placed,
        out_specs=(
            P(("dp", "expert"), None, None),
            P(("dp", "expert"), None),
            P("expert", None, "dp", None),
        ),
        check_vma=False,
    )
```

```python
import jax
import jax.numpy as jnp
from jax import lax
from jax.sharding import PartitionSpec as P

EXPERTS = 64
CAP = 16
HOT = 16


def slot_of_route(experts, replicas, flat_slots):
    slot_count = flat_slots.shape[0]
    ordering = jnp.arange(slot_count, dtype=jnp.int32)
    same_expert = flat_slots[:, None] == flat_slots[None, :]
    replica_rank = jnp.sum(
        (same_expert & (ordering[None, :] < ordering[:, None])).astype(jnp.int32), axis=1
    )
    matches = (experts.reshape(-1)[:, None] == flat_slots[None, :]) & (
        replicas.reshape(-1)[:, None] == replica_rank[None, :]
    )
    return jnp.sum(jnp.where(matches, ordering[None, :], 0), axis=1)


def buffer_places(experts, replicas, flat_slots, capacity):
    destination = slot_of_route(experts, replicas, flat_slots)
    route_count = destination.shape[0]
    ordering = jnp.arange(route_count, dtype=jnp.int32)
    earlier = (destination[:, None] == destination[None, :]) & (ordering[None, :] < ordering[:, None])
    position = jnp.sum(earlier.astype(jnp.int32), axis=1)
    return destination * capacity + position


def route_of_place(places, length):
    route_count = places.shape[0]
    return (
        jnp.full((length,), route_count, jnp.int32)
        .at[places]
        .set(jnp.arange(route_count, dtype=jnp.int32))
    )


def exchange_sum(x, axis, count):
    pieces = lax.all_to_all(x.reshape(count, -1), axis, split_axis=0, concat_axis=0, tiled=True)
    own_total = jnp.sum(pieces, axis=0)
    copies = jnp.broadcast_to(own_total[None], pieces.shape)
    totals = lax.all_to_all(copies, axis, split_axis=0, concat_axis=0, tiled=True)
    return totals.reshape(x.shape)


def per_device(out_grad, hidden, gate, route_expert, route_replica, slot_expert, down_weight):
    tok_rows, chosen_count = gate.shape
    model_width = out_grad.shape[1]
    hidden_width = hidden.shape[2]
    groups, slots = slot_expert.shape
    flat_slots = slot_expert.reshape(-1)
    capacity = CAP
    block_rows = slots * capacity
    length = groups * block_rows
    route_count = tok_rows * chosen_count
    own_index = lax.axis_index("expert")
    places = buffer_places(route_expert, route_replica, flat_slots, capacity)
    source_route = route_of_place(places, length)
    hidden_rows = jnp.concatenate(
        [hidden.reshape(route_count, hidden_width), jnp.zeros((1, hidden_width), hidden.dtype)],
        axis=0,
    )
    gate_rows = jnp.concatenate([gate.reshape(route_count), jnp.zeros((1,), gate.dtype)])
    sent_hidden = hidden_rows[source_route].reshape(groups, block_rows, hidden_width)
    sent_gate = gate_rows[source_route].reshape(groups, block_rows)
    padded_grad = jnp.concatenate([out_grad, jnp.zeros((1, model_width), out_grad.dtype)], axis=0)
    token_rows = jnp.where(source_route < route_count, source_route // chosen_count, tok_rows)
    sent_grad = padded_grad[token_rows].reshape(groups, block_rows, model_width)
    lane = 128
    gate_block = jnp.pad(sent_gate[..., None], ((0, 0), (0, 0), (0, lane - 1)))
    sent = jnp.concatenate([sent_grad, sent_hidden, gate_block], axis=-1)
    got = lax.all_to_all(sent, "expert", split_axis=0, concat_axis=0, tiled=True)
    got_grad = got[..., :model_width]
    got_hidden = got[..., model_width : model_width + hidden_width]
    got_gate = got[..., model_width + hidden_width]
    weights = down_weight[0]
    grad_four = got_grad.reshape(groups, slots, capacity, model_width)
    hidden_four = got_hidden.reshape(groups, slots, capacity, hidden_width)
    gate_four = got_gate.reshape(groups, slots, capacity).astype(jnp.float32)[..., None]
    projected = jnp.einsum("xscd,sfd->xscf", grad_four, weights, preferred_element_type=jnp.float32)
    back_rows = (
        (gate_four * projected).astype(jnp.bfloat16).reshape(groups, block_rows, hidden_width)
    )
    back_gate = (
        jnp.sum(hidden_four.astype(jnp.float32) * projected, axis=-1)
        .astype(jnp.bfloat16)
        .reshape(groups, block_rows)
    )
    back_block = jnp.pad(back_gate[..., None], ((0, 0), (0, 0), (0, lane - 1)))
    came = lax.all_to_all(
        jnp.concatenate([back_rows, back_block], axis=-1),
        "expert",
        split_axis=0,
        concat_axis=0,
        tiled=True,
    )
    came_rows = came[..., :hidden_width]
    came_gate = came[..., hidden_width]
    d_hidden = came_rows.reshape(length, hidden_width)[places].reshape(
        tok_rows, chosen_count, hidden_width
    )
    d_gate = came_gate.reshape(length)[places].reshape(tok_rows, chosen_count)
    scaled = (gate_four * hidden_four.astype(jnp.float32)).astype(jnp.bfloat16)
    partial_value = jnp.einsum(
        "xscf,xscd->sfd", scaled, grad_four, preferred_element_type=jnp.float32
    )
    group_sum = lax.psum_scatter(partial_value, "dp", scatter_dimension=1, tiled=True)
    own_slots = lax.dynamic_slice_in_dim(flat_slots, own_index * slots, slots)
    expert_ids = jnp.arange(EXPERTS, dtype=jnp.int32)
    copies = jnp.sum((flat_slots[:, None] == expert_ids[None, :]).astype(jnp.int32), axis=0)
    is_hot = copies >= 2
    hot_rank = jnp.cumsum(is_hot.astype(jnp.int32)) - 1
    picks = own_slots[:, None] == expert_ids[None, :]
    slot_hot = jnp.any(picks & is_hot[None, :], axis=1)
    slot_rank = jnp.sum(jnp.where(picks, hot_rank[None, :], 0), axis=1)
    member = (slot_rank[:, None] == jnp.arange(HOT, dtype=jnp.int32)[None, :]) & slot_hot[:, None]
    hot_table = jnp.sum(jnp.where(member[:, :, None, None], group_sum[:, None], 0.0), axis=0)
    hot_total = exchange_sum(hot_table, "expert", lax.axis_size("expert"))
    from_table = jnp.sum(jnp.where(member[:, :, None, None], hot_total[None], 0.0), axis=1)
    d_weight = jnp.where(slot_hot[:, None, None], from_table, group_sum)[None]
    return (d_hidden, d_gate, d_weight)


def solution(mesh):
    placed = (
        P(("dp", "expert"), None),
        P(("dp", "expert"), None, None),
        P(("dp", "expert"), None),
        P(("dp", "expert"), None),
        P(("dp", "expert"), None),
        P(),
        P("expert", None, None, None),
    )
    return jax.shard_map(
        per_device,
        mesh=mesh,
        in_specs=placed,
        out_specs=(
            P(("dp", "expert"), None, None),
            P(("dp", "expert"), None),
            P("expert", None, "dp", None),
        ),
        check_vma=False,
    )
```

```python
import jax
import jax.numpy as jnp
from jax import lax
from jax.sharding import PartitionSpec as P

EXPERTS = 64
CAP = 16
HOT = 16


def slot_of_route(experts, replicas, flat_slots):
    slot_count = flat_slots.shape[0]
    ordering = jnp.arange(slot_count, dtype=jnp.int32)
    same_expert = flat_slots[:, None] == flat_slots[None, :]
    replica_rank = jnp.sum(
        (same_expert & (ordering[None, :] < ordering[:, None])).astype(jnp.int32), axis=1
    )
    matches = (experts.reshape(-1)[:, None] == flat_slots[None, :]) & (
        replicas.reshape(-1)[:, None] == replica_rank[None, :]
    )
    return jnp.sum(jnp.where(matches, ordering[None, :], 0), axis=1)


def buffer_places(experts, replicas, flat_slots, capacity):
    destination = slot_of_route(experts, replicas, flat_slots)
    route_count = destination.shape[0]
    ordering = jnp.arange(route_count, dtype=jnp.int32)
    earlier = (destination[:, None] == destination[None, :]) & (ordering[None, :] < ordering[:, None])
    position = jnp.sum(earlier.astype(jnp.int32), axis=1)
    return destination * capacity + position


def exchange_sum(x, axis, count):
    pieces = lax.all_to_all(x.reshape(count, -1), axis, split_axis=0, concat_axis=0, tiled=True)
    own_total = jnp.sum(pieces, axis=0)
    copies = jnp.broadcast_to(own_total[None], pieces.shape)
    totals = lax.all_to_all(copies, axis, split_axis=0, concat_axis=0, tiled=True)
    return totals.reshape(x.shape)


def per_device(out_grad, hidden, gate, route_expert, route_replica, slot_expert, down_weight):
    tok_rows, chosen_count = gate.shape
    model_width = out_grad.shape[1]
    hidden_width = hidden.shape[2]
    groups, slots = slot_expert.shape
    flat_slots = slot_expert.reshape(-1)
    capacity = CAP
    block_rows = slots * capacity
    length = groups * block_rows
    route_count = tok_rows * chosen_count
    own_index = lax.axis_index("expert")
    places = buffer_places(route_expert, route_replica, flat_slots, capacity)
    lane = 128
    spots = jnp.arange(length, dtype=jnp.int32)
    chosen = places[None, :] == spots[:, None]
    pick_route = chosen.astype(jnp.bfloat16)
    pick_token = jnp.sum(
        chosen.reshape(length, tok_rows, chosen_count).astype(jnp.int32), axis=2
    ).astype(jnp.bfloat16)
    route_table = jnp.concatenate(
        [
            hidden.reshape(route_count, hidden_width),
            jnp.pad(gate.reshape(route_count, 1), ((0, 0), (0, lane - 1))),
        ],
        axis=1,
    )
    sent_grad = jnp.dot(pick_token, out_grad, preferred_element_type=jnp.float32)
    sent_route = jnp.dot(pick_route, route_table, preferred_element_type=jnp.float32)
    sent = jnp.concatenate(
        [sent_grad.astype(jnp.bfloat16), sent_route.astype(jnp.bfloat16)], axis=1
    ).reshape(groups, block_rows, model_width + hidden_width + lane)
    got = lax.all_to_all(sent, "expert", split_axis=0, concat_axis=0, tiled=True)
    got_grad = got[..., :model_width]
    got_hidden = got[..., model_width : model_width + hidden_width]
    got_gate = got[..., model_width + hidden_width]
    weights = down_weight[0]
    grad_four = got_grad.reshape(groups, slots, capacity, model_width)
    hidden_four = got_hidden.reshape(groups, slots, capacity, hidden_width)
    gate_four = got_gate.reshape(groups, slots, capacity).astype(jnp.float32)[..., None]
    projected = jnp.einsum("xscd,sfd->xscf", grad_four, weights, preferred_element_type=jnp.float32)
    back_rows = (
        (gate_four * projected).astype(jnp.bfloat16).reshape(groups, block_rows, hidden_width)
    )
    back_gate = (
        jnp.sum(hidden_four.astype(jnp.float32) * projected, axis=-1)
        .astype(jnp.bfloat16)
        .reshape(groups, block_rows)
    )
    back_block = jnp.pad(back_gate[..., None], ((0, 0), (0, 0), (0, lane - 1)))
    came = lax.all_to_all(
        jnp.concatenate([back_rows, back_block], axis=-1),
        "expert",
        split_axis=0,
        concat_axis=0,
        tiled=True,
    )
    came_rows = came[..., :hidden_width]
    came_gate = came[..., hidden_width]
    d_hidden = came_rows.reshape(length, hidden_width)[places].reshape(
        tok_rows, chosen_count, hidden_width
    )
    d_gate = came_gate.reshape(length)[places].reshape(tok_rows, chosen_count)
    scaled = (gate_four * hidden_four.astype(jnp.float32)).astype(jnp.bfloat16)
    partial_value = jnp.einsum(
        "xscf,xscd->sfd", scaled, grad_four, preferred_element_type=jnp.float32
    )
    group_sum = lax.psum_scatter(partial_value, "dp", scatter_dimension=1, tiled=True)
    own_slots = lax.dynamic_slice_in_dim(flat_slots, own_index * slots, slots)
    expert_ids = jnp.arange(EXPERTS, dtype=jnp.int32)
    copies = jnp.sum((flat_slots[:, None] == expert_ids[None, :]).astype(jnp.int32), axis=0)
    is_hot = copies >= 2
    hot_rank = jnp.cumsum(is_hot.astype(jnp.int32)) - 1
    picks = own_slots[:, None] == expert_ids[None, :]
    slot_hot = jnp.any(picks & is_hot[None, :], axis=1)
    slot_rank = jnp.sum(jnp.where(picks, hot_rank[None, :], 0), axis=1)
    member = (slot_rank[:, None] == jnp.arange(HOT, dtype=jnp.int32)[None, :]) & slot_hot[:, None]
    hot_table = jnp.sum(jnp.where(member[:, :, None, None], group_sum[:, None], 0.0), axis=0)
    hot_total = exchange_sum(hot_table, "expert", lax.axis_size("expert"))
    from_table = jnp.sum(jnp.where(member[:, :, None, None], hot_total[None], 0.0), axis=1)
    d_weight = jnp.where(slot_hot[:, None, None], from_table, group_sum)[None]
    return (d_hidden, d_gate, d_weight)


def solution(mesh):
    placed = (
        P(("dp", "expert"), None),
        P(("dp", "expert"), None, None),
        P(("dp", "expert"), None),
        P(("dp", "expert"), None),
        P(("dp", "expert"), None),
        P(),
        P("expert", None, None, None),
    )
    return jax.shard_map(
        per_device,
        mesh=mesh,
        in_specs=placed,
        out_specs=(
            P(("dp", "expert"), None, None),
            P(("dp", "expert"), None),
            P("expert", None, "dp", None),
        ),
        check_vma=False,
    )
```

```python
import jax
import jax.numpy as jnp
from jax import lax
from jax.sharding import PartitionSpec as P

EXPERTS = 64
CAP = 16
HOT = 16


def slot_of_route(experts, replicas, flat_slots):
    slot_count = flat_slots.shape[0]
    ordering = jnp.arange(slot_count, dtype=jnp.int32)
    same_expert = flat_slots[:, None] == flat_slots[None, :]
    replica_rank = jnp.sum(
        (same_expert & (ordering[None, :] < ordering[:, None])).astype(jnp.int32), axis=1
    )
    matches = (experts.reshape(-1)[:, None] == flat_slots[None, :]) & (
        replicas.reshape(-1)[:, None] == replica_rank[None, :]
    )
    return jnp.sum(jnp.where(matches, ordering[None, :], 0), axis=1)


def buffer_places(experts, replicas, flat_slots, capacity):
    destination = slot_of_route(experts, replicas, flat_slots)
    route_count = destination.shape[0]
    ordering = jnp.arange(route_count, dtype=jnp.int32)
    earlier = (destination[:, None] == destination[None, :]) & (ordering[None, :] < ordering[:, None])
    position = jnp.sum(earlier.astype(jnp.int32), axis=1)
    return destination * capacity + position


def exchange_sum(x, axis, count):
    pieces = lax.all_to_all(x.reshape(count, -1), axis, split_axis=0, concat_axis=0, tiled=True)
    own_total = jnp.sum(pieces, axis=0)
    copies = jnp.broadcast_to(own_total[None], pieces.shape)
    totals = lax.all_to_all(copies, axis, split_axis=0, concat_axis=0, tiled=True)
    return totals.reshape(x.shape)


def per_device(out_grad, hidden, gate, route_expert, route_replica, slot_expert, down_weight):
    tok_rows, chosen_count = gate.shape
    model_width = out_grad.shape[1]
    hidden_width = hidden.shape[2]
    groups, slots = slot_expert.shape
    flat_slots = slot_expert.reshape(-1)
    capacity = CAP
    block_rows = slots * capacity
    length = groups * block_rows
    route_count = tok_rows * chosen_count
    own_index = lax.axis_index("expert")
    places = buffer_places(route_expert, route_replica, flat_slots, capacity)
    lane = 128
    spots = jnp.arange(length, dtype=jnp.int32)
    chosen = places[None, :] == spots[:, None]
    pick_route = chosen.astype(jnp.bfloat16)
    route_token = (
        jnp.arange(route_count, dtype=jnp.int32)[:, None] // chosen_count
        == jnp.arange(tok_rows, dtype=jnp.int32)[None, :]
    ).astype(jnp.bfloat16)
    pick_token = jnp.dot(pick_route, route_token, preferred_element_type=jnp.float32).astype(
        jnp.bfloat16
    )
    route_table = jnp.concatenate(
        [
            hidden.reshape(route_count, hidden_width),
            jnp.pad(gate.reshape(route_count, 1), ((0, 0), (0, lane - 1))),
        ],
        axis=1,
    )
    block_table = jnp.concatenate(
        [
            jnp.pad(out_grad, ((0, 0), (0, hidden_width + lane))),
            jnp.pad(route_table, ((0, 0), (model_width, 0))),
        ],
        axis=0,
    )
    picks = jnp.concatenate([pick_token, pick_route], axis=1)
    sent = (
        jnp.dot(picks, block_table, preferred_element_type=jnp.float32)
        .astype(jnp.bfloat16)
        .reshape(groups, block_rows, model_width + hidden_width + lane)
    )
    got = lax.all_to_all(sent, "expert", split_axis=0, concat_axis=0, tiled=True)
    got_grad = got[..., :model_width]
    got_hidden = got[..., model_width : model_width + hidden_width]
    got_gate = got[..., model_width + hidden_width]
    weights = down_weight[0]
    grad_four = got_grad.reshape(groups, slots, capacity, model_width)
    hidden_four = got_hidden.reshape(groups, slots, capacity, hidden_width)
    gate_four = got_gate.reshape(groups, slots, capacity).astype(jnp.float32)[..., None]
    projected = jnp.einsum("xscd,sfd->xscf", grad_four, weights, preferred_element_type=jnp.float32)
    back_rows = (
        (gate_four * projected).astype(jnp.bfloat16).reshape(groups, block_rows, hidden_width)
    )
    back_gate = (
        jnp.sum(hidden_four.astype(jnp.float32) * projected, axis=-1)
        .astype(jnp.bfloat16)
        .reshape(groups, block_rows)
    )
    back_block = jnp.pad(back_gate[..., None], ((0, 0), (0, 0), (0, lane - 1)))
    came = lax.all_to_all(
        jnp.concatenate([back_rows, back_block], axis=-1),
        "expert",
        split_axis=0,
        concat_axis=0,
        tiled=True,
    )
    came_rows = came[..., :hidden_width]
    came_gate = came[..., hidden_width]
    d_hidden = came_rows.reshape(length, hidden_width)[places].reshape(
        tok_rows, chosen_count, hidden_width
    )
    d_gate = came_gate.reshape(length)[places].reshape(tok_rows, chosen_count)
    scaled = (gate_four * hidden_four.astype(jnp.float32)).astype(jnp.bfloat16)
    partial_value = jnp.einsum(
        "xscf,xscd->sfd", scaled, grad_four, preferred_element_type=jnp.float32
    )
    group_sum = lax.psum_scatter(partial_value, "dp", scatter_dimension=1, tiled=True)
    own_slots = lax.dynamic_slice_in_dim(flat_slots, own_index * slots, slots)
    expert_ids = jnp.arange(EXPERTS, dtype=jnp.int32)
    copies = jnp.sum((flat_slots[:, None] == expert_ids[None, :]).astype(jnp.int32), axis=0)
    is_hot = copies >= 2
    hot_rank = jnp.cumsum(is_hot.astype(jnp.int32)) - 1
    picks = own_slots[:, None] == expert_ids[None, :]
    slot_hot = jnp.any(picks & is_hot[None, :], axis=1)
    slot_rank = jnp.sum(jnp.where(picks, hot_rank[None, :], 0), axis=1)
    member = (slot_rank[:, None] == jnp.arange(HOT, dtype=jnp.int32)[None, :]) & slot_hot[:, None]
    hot_table = jnp.sum(jnp.where(member[:, :, None, None], group_sum[:, None], 0.0), axis=0)
    hot_total = exchange_sum(hot_table, "expert", lax.axis_size("expert"))
    from_table = jnp.sum(jnp.where(member[:, :, None, None], hot_total[None], 0.0), axis=1)
    d_weight = jnp.where(slot_hot[:, None, None], from_table, group_sum)[None]
    return (d_hidden, d_gate, d_weight)


def solution(mesh):
    placed = (
        P(("dp", "expert"), None),
        P(("dp", "expert"), None, None),
        P(("dp", "expert"), None),
        P(("dp", "expert"), None),
        P(("dp", "expert"), None),
        P(),
        P("expert", None, None, None),
    )
    return jax.shard_map(
        per_device,
        mesh=mesh,
        in_specs=placed,
        out_specs=(
            P(("dp", "expert"), None, None),
            P(("dp", "expert"), None),
            P("expert", None, "dp", None),
        ),
        check_vma=False,
    )
```

```python
import jax
import jax.numpy as jnp
from jax import lax
from jax.sharding import PartitionSpec as P

EXPERTS = 64
CAP = 16
HOT = 16


def slot_of_route(experts, replicas, flat_slots):
    slot_count = flat_slots.shape[0]
    ordering = jnp.arange(slot_count, dtype=jnp.int32)
    same_expert = flat_slots[:, None] == flat_slots[None, :]
    replica_rank = jnp.sum(
        (same_expert & (ordering[None, :] < ordering[:, None])).astype(jnp.int32), axis=1
    )
    matches = (experts.reshape(-1)[:, None] == flat_slots[None, :]) & (
        replicas.reshape(-1)[:, None] == replica_rank[None, :]
    )
    return jnp.sum(jnp.where(matches, ordering[None, :], 0), axis=1)


def buffer_places(experts, replicas, flat_slots, capacity):
    destination = slot_of_route(experts, replicas, flat_slots)
    route_count = destination.shape[0]
    ordering = jnp.arange(route_count, dtype=jnp.int32)
    earlier = (destination[:, None] == destination[None, :]) & (ordering[None, :] < ordering[:, None])
    position = jnp.sum(earlier.astype(jnp.int32), axis=1)
    return destination * capacity + position


def exchange_sum(x, axis, count):
    pieces = lax.all_to_all(
        x.reshape(count, 8, -1).astype(jnp.bfloat16), axis, split_axis=0, concat_axis=0, tiled=True
    )
    own_total = jnp.sum(pieces.astype(jnp.float32), axis=0)
    copies = jnp.broadcast_to(own_total[None], pieces.shape)
    totals = lax.all_to_all(copies, axis, split_axis=0, concat_axis=0, tiled=True)
    return totals.reshape(x.shape)


def per_device(out_grad, hidden, gate, route_expert, route_replica, slot_expert, down_weight):
    tok_rows, chosen_count = gate.shape
    model_width = out_grad.shape[1]
    hidden_width = hidden.shape[2]
    groups, slots = slot_expert.shape
    flat_slots = slot_expert.reshape(-1)
    capacity = CAP
    block_rows = slots * capacity
    length = groups * block_rows
    route_count = tok_rows * chosen_count
    own_index = lax.axis_index("expert")
    places = buffer_places(route_expert, route_replica, flat_slots, capacity)
    lane = 128
    spots = jnp.arange(length, dtype=jnp.int32)
    chosen = places[None, :] == spots[:, None]
    pick_route = chosen.astype(jnp.bfloat16)
    route_token = (
        jnp.arange(route_count, dtype=jnp.int32)[:, None] // chosen_count
        == jnp.arange(tok_rows, dtype=jnp.int32)[None, :]
    ).astype(jnp.bfloat16)
    pick_token = jnp.dot(pick_route, route_token, preferred_element_type=jnp.float32).astype(
        jnp.bfloat16
    )
    route_table = jnp.concatenate(
        [
            hidden.reshape(route_count, hidden_width),
            jnp.pad(gate.reshape(route_count, 1), ((0, 0), (0, lane - 1))),
        ],
        axis=1,
    )
    block_table = jnp.concatenate(
        [
            jnp.pad(out_grad, ((0, 0), (0, hidden_width + lane))),
            jnp.pad(route_table, ((0, 0), (model_width, 0))),
        ],
        axis=0,
    )
    picks = jnp.concatenate([pick_token, pick_route], axis=1)
    sent = (
        jnp.dot(picks, block_table, preferred_element_type=jnp.float32)
        .astype(jnp.bfloat16)
        .reshape(groups, block_rows, model_width + hidden_width + lane)
    )
    got = lax.all_to_all(sent, "expert", split_axis=0, concat_axis=0, tiled=True)
    got_grad = got[..., :model_width]
    got_hidden = got[..., model_width : model_width + hidden_width]
    got_gate = got[..., model_width + hidden_width]
    weights = down_weight[0]
    grad_four = got_grad.reshape(groups, slots, capacity, model_width)
    hidden_four = got_hidden.reshape(groups, slots, capacity, hidden_width)
    gate_four = got_gate.reshape(groups, slots, capacity).astype(jnp.float32)[..., None]
    projected = jnp.einsum("xscd,sfd->xscf", grad_four, weights, preferred_element_type=jnp.float32)
    back_rows = (
        (gate_four * projected).astype(jnp.bfloat16).reshape(groups, block_rows, hidden_width)
    )
    back_gate = (
        jnp.sum(hidden_four.astype(jnp.float32) * projected, axis=-1)
        .astype(jnp.bfloat16)
        .reshape(groups, block_rows)
    )
    back_block = jnp.pad(back_gate[..., None], ((0, 0), (0, 0), (0, lane - 1)))
    came = lax.all_to_all(
        jnp.concatenate([back_rows, back_block], axis=-1),
        "expert",
        split_axis=0,
        concat_axis=0,
        tiled=True,
    )
    came_rows = came[..., :hidden_width]
    came_gate = came[..., hidden_width]
    d_hidden = came_rows.reshape(length, hidden_width)[places].reshape(
        tok_rows, chosen_count, hidden_width
    )
    d_gate = came_gate.reshape(length)[places].reshape(tok_rows, chosen_count)
    scaled = (gate_four * hidden_four.astype(jnp.float32)).astype(jnp.bfloat16)
    partial_value = jnp.einsum(
        "xscf,xscd->sfd", scaled, grad_four, preferred_element_type=jnp.float32
    )
    group_sum = lax.psum_scatter(partial_value, "dp", scatter_dimension=1, tiled=True)
    own_slots = lax.dynamic_slice_in_dim(flat_slots, own_index * slots, slots)
    expert_ids = jnp.arange(EXPERTS, dtype=jnp.int32)
    copies = jnp.sum((flat_slots[:, None] == expert_ids[None, :]).astype(jnp.int32), axis=0)
    is_hot = copies >= 2
    hot_rank = jnp.cumsum(is_hot.astype(jnp.int32)) - 1
    picks = own_slots[:, None] == expert_ids[None, :]
    slot_hot = jnp.any(picks & is_hot[None, :], axis=1)
    slot_rank = jnp.sum(jnp.where(picks, hot_rank[None, :], 0), axis=1)
    member = (slot_rank[:, None] == jnp.arange(HOT, dtype=jnp.int32)[None, :]) & slot_hot[:, None]
    hot_table = jnp.sum(jnp.where(member[:, :, None, None], group_sum[:, None], 0.0), axis=0)
    hot_total = exchange_sum(hot_table, "expert", lax.axis_size("expert"))
    from_table = hot_total[jnp.clip(slot_rank, 0, HOT - 1)]
    d_weight = jnp.where(slot_hot[:, None, None], from_table, group_sum)[None]
    return (d_hidden, d_gate, d_weight)


def solution(mesh):
    placed = (
        P(("dp", "expert"), None),
        P(("dp", "expert"), None, None),
        P(("dp", "expert"), None),
        P(("dp", "expert"), None),
        P(("dp", "expert"), None),
        P(),
        P("expert", None, None, None),
    )
    return jax.shard_map(
        per_device,
        mesh=mesh,
        in_specs=placed,
        out_specs=(
            P(("dp", "expert"), None, None),
            P(("dp", "expert"), None),
            P("expert", None, "dp", None),
        ),
        check_vma=False,
    )
```

```python
import jax
import jax.numpy as jnp
from jax import lax
from jax.sharding import PartitionSpec as P

EXPERTS = 64
CAP = 16
HOT = 16


def slot_of_route(experts, replicas, flat_slots):
    slot_count = flat_slots.shape[0]
    ordering = jnp.arange(slot_count, dtype=jnp.int32)
    same_expert = flat_slots[:, None] == flat_slots[None, :]
    replica_rank = jnp.sum(
        (same_expert & (ordering[None, :] < ordering[:, None])).astype(jnp.int32), axis=1
    )
    matches = (experts.reshape(-1)[:, None] == flat_slots[None, :]) & (
        replicas.reshape(-1)[:, None] == replica_rank[None, :]
    )
    return jnp.sum(jnp.where(matches, ordering[None, :], 0), axis=1)


def buffer_places(experts, replicas, flat_slots, capacity):
    destination = slot_of_route(experts, replicas, flat_slots)
    route_count = destination.shape[0]
    ordering = jnp.arange(route_count, dtype=jnp.int32)
    earlier = (destination[:, None] == destination[None, :]) & (ordering[None, :] < ordering[:, None])
    position = jnp.sum(earlier.astype(jnp.int32), axis=1)
    return destination * capacity + position


def exchange_sum(x, axis, count):
    pieces = lax.all_to_all(
        x.reshape(count, 8, -1), axis, split_axis=0, concat_axis=0, tiled=True
    )
    own_total = jnp.sum(pieces, axis=0)
    copies = jnp.broadcast_to(own_total[None], pieces.shape)
    totals = lax.all_to_all(copies, axis, split_axis=0, concat_axis=0, tiled=True)
    return totals.reshape(x.shape)


def per_device(out_grad, hidden, gate, route_expert, route_replica, slot_expert, down_weight):
    tok_rows, chosen_count = gate.shape
    model_width = out_grad.shape[1]
    hidden_width = hidden.shape[2]
    groups, slots = slot_expert.shape
    flat_slots = slot_expert.reshape(-1)
    capacity = CAP
    block_rows = slots * capacity
    length = groups * block_rows
    route_count = tok_rows * chosen_count
    own_index = lax.axis_index("expert")
    places = buffer_places(route_expert, route_replica, flat_slots, capacity)
    lane = 128
    spots = jnp.arange(length, dtype=jnp.int32)
    chosen = places[None, :] == spots[:, None]
    pick_route = chosen.astype(jnp.bfloat16)
    route_token = (
        jnp.arange(route_count, dtype=jnp.int32)[:, None] // chosen_count
        == jnp.arange(tok_rows, dtype=jnp.int32)[None, :]
    ).astype(jnp.bfloat16)
    pick_token = jnp.dot(pick_route, route_token, preferred_element_type=jnp.float32).astype(
        jnp.bfloat16
    )
    route_table = jnp.concatenate(
        [
            hidden.reshape(route_count, hidden_width),
            jnp.pad(gate.reshape(route_count, 1), ((0, 0), (0, lane - 1))),
        ],
        axis=1,
    )
    block_table = jnp.concatenate(
        [
            jnp.pad(out_grad, ((0, 0), (0, hidden_width + lane))),
            jnp.pad(route_table, ((0, 0), (model_width, 0))),
        ],
        axis=0,
    )
    picks = jnp.concatenate([pick_token, pick_route], axis=1)
    sent = (
        jnp.dot(picks, block_table, preferred_element_type=jnp.float32)
        .astype(jnp.bfloat16)
        .reshape(groups, block_rows, model_width + hidden_width + lane)
    )
    got = lax.all_to_all(sent, "expert", split_axis=0, concat_axis=0, tiled=True)
    got_grad = got[..., :model_width]
    got_hidden = got[..., model_width : model_width + hidden_width]
    got_gate = got[..., model_width + hidden_width]
    weights = down_weight[0]
    grad_four = got_grad.reshape(groups, slots, capacity, model_width)
    hidden_four = got_hidden.reshape(groups, slots, capacity, hidden_width)
    gate_four = got_gate.reshape(groups, slots, capacity).astype(jnp.float32)[..., None]
    projected = jnp.einsum("xscd,sfd->xscf", grad_four, weights, preferred_element_type=jnp.float32)
    back_rows = (
        (gate_four * projected).astype(jnp.bfloat16).reshape(groups, block_rows, hidden_width)
    )
    back_gate = (
        jnp.sum(hidden_four.astype(jnp.float32) * projected, axis=-1)
        .astype(jnp.bfloat16)
        .reshape(groups, block_rows)
    )
    back_block = jnp.pad(back_gate[..., None], ((0, 0), (0, 0), (0, lane - 1)))
    came = lax.all_to_all(
        jnp.concatenate([back_rows, back_block], axis=-1),
        "expert",
        split_axis=0,
        concat_axis=0,
        tiled=True,
    )
    came_rows = came[..., :hidden_width]
    came_gate = came[..., hidden_width]
    d_hidden = came_rows.reshape(length, hidden_width)[places].reshape(
        tok_rows, chosen_count, hidden_width
    )
    d_gate = came_gate.reshape(length)[places].reshape(tok_rows, chosen_count)
    scaled = (gate_four * hidden_four.astype(jnp.float32)).astype(jnp.bfloat16)
    partial_value = jnp.einsum(
        "xscf,xscd->sfd", scaled, grad_four, preferred_element_type=jnp.float32
    )
    group_sum = lax.psum_scatter(partial_value, "dp", scatter_dimension=1, tiled=True)
    own_slots = lax.dynamic_slice_in_dim(flat_slots, own_index * slots, slots)
    expert_ids = jnp.arange(EXPERTS, dtype=jnp.int32)
    copies = jnp.sum((flat_slots[:, None] == expert_ids[None, :]).astype(jnp.int32), axis=0)
    is_hot = copies >= 2
    hot_rank = jnp.cumsum(is_hot.astype(jnp.int32)) - 1
    picks = own_slots[:, None] == expert_ids[None, :]
    slot_hot = jnp.any(picks & is_hot[None, :], axis=1)
    slot_rank = jnp.sum(jnp.where(picks, hot_rank[None, :], 0), axis=1)
    member = (slot_rank[:, None] == jnp.arange(HOT, dtype=jnp.int32)[None, :]) & slot_hot[:, None]
    expert_count = lax.axis_size("expert")
    halves = expert_count // HOT
    chunk_rows = 8
    chunked = group_sum.reshape(slots, halves, chunk_rows, -1)
    hot_table = jnp.sum(
        jnp.where(member[:, :, None, None, None], chunked[:, None], 0.0), axis=0
    ).reshape(expert_count, chunk_rows, -1)
    hot_total = exchange_sum(hot_table, "expert", expert_count).reshape(
        HOT, halves, chunk_rows, -1
    )
    from_table = hot_total[jnp.clip(slot_rank, 0, HOT - 1)].reshape(group_sum.shape)
    d_weight = jnp.where(slot_hot[:, None, None], from_table, group_sum)[None]
    return (d_hidden, d_gate, d_weight)


def solution(mesh):
    placed = (
        P(("dp", "expert"), None),
        P(("dp", "expert"), None, None),
        P(("dp", "expert"), None),
        P(("dp", "expert"), None),
        P(("dp", "expert"), None),
        P(),
        P("expert", None, None, None),
    )
    return jax.shard_map(
        per_device,
        mesh=mesh,
        in_specs=placed,
        out_specs=(
            P(("dp", "expert"), None, None),
            P(("dp", "expert"), None),
            P("expert", None, "dp", None),
        ),
        check_vma=False,
    )
```

```python
import jax
import jax.numpy as jnp
from jax import lax
from jax.sharding import PartitionSpec as P

EXPERTS = 64
CAP = 16
HOT = 16


def slot_of_route(experts, replicas, flat_slots):
    slot_count = flat_slots.shape[0]
    ordering = jnp.arange(slot_count, dtype=jnp.int32)
    same_expert = flat_slots[:, None] == flat_slots[None, :]
    replica_rank = jnp.sum(
        (same_expert & (ordering[None, :] < ordering[:, None])).astype(jnp.int32), axis=1
    )
    matches = (experts.reshape(-1)[:, None] == flat_slots[None, :]) & (
        replicas.reshape(-1)[:, None] == replica_rank[None, :]
    )
    return jnp.sum(jnp.where(matches, ordering[None, :], 0), axis=1)


def buffer_places(experts, replicas, flat_slots, capacity):
    destination = slot_of_route(experts, replicas, flat_slots)
    route_count = destination.shape[0]
    ordering = jnp.arange(route_count, dtype=jnp.int32)
    earlier = (destination[:, None] == destination[None, :]) & (ordering[None, :] < ordering[:, None])
    position = jnp.sum(earlier.astype(jnp.int32), axis=1)
    return destination * capacity + position


def exchange_sum(x, axis, count):
    pieces = lax.all_to_all(
        x.reshape(count, 8, -1).astype(jnp.bfloat16), axis, split_axis=0, concat_axis=0, tiled=True
    )
    own_total = jnp.sum(pieces.astype(jnp.float32), axis=0)
    copies = jnp.broadcast_to(own_total[None], pieces.shape)
    totals = lax.all_to_all(copies, axis, split_axis=0, concat_axis=0, tiled=True)
    return totals.reshape(x.shape)


def per_device(out_grad, hidden, gate, route_expert, route_replica, slot_expert, down_weight):
    tok_rows, chosen_count = gate.shape
    model_width = out_grad.shape[1]
    hidden_width = hidden.shape[2]
    groups, slots = slot_expert.shape
    flat_slots = slot_expert.reshape(-1)
    capacity = CAP
    block_rows = slots * capacity
    length = groups * block_rows
    route_count = tok_rows * chosen_count
    own_index = lax.axis_index("expert")
    places = buffer_places(route_expert, route_replica, flat_slots, capacity)
    lane = 128
    spots = jnp.arange(length, dtype=jnp.int32)
    chosen = places[None, :] == spots[:, None]
    pick_route = chosen.astype(jnp.bfloat16)
    token_plus = jnp.arange(route_count, dtype=jnp.int32) // chosen_count + 1
    token_of_spot = jnp.sum(jnp.where(chosen, token_plus[None, :], 0), axis=1)
    pick_token = (
        token_of_spot[:, None] == jnp.arange(1, tok_rows + 1, dtype=jnp.int32)[None, :]
    ).astype(jnp.bfloat16)
    route_table = jnp.concatenate(
        [
            hidden.reshape(route_count, hidden_width),
            jnp.pad(gate.reshape(route_count, 1), ((0, 0), (0, lane - 1))),
        ],
        axis=1,
    )
    block_table = jnp.concatenate(
        [
            jnp.pad(out_grad, ((0, 0), (0, hidden_width + lane))),
            jnp.pad(route_table, ((0, 0), (model_width, 0))),
        ],
        axis=0,
    )
    picks = jnp.concatenate([pick_token, pick_route], axis=1)
    sent = (
        jnp.dot(picks, block_table, preferred_element_type=jnp.float32)
        .astype(jnp.bfloat16)
        .reshape(groups, block_rows, model_width + hidden_width + lane)
    )
    got = lax.all_to_all(sent, "expert", split_axis=0, concat_axis=0, tiled=True)
    got_grad = got[..., :model_width]
    got_hidden = got[..., model_width : model_width + hidden_width]
    got_gate = got[..., model_width + hidden_width]
    weights = down_weight[0]
    grad_four = got_grad.reshape(groups, slots, capacity, model_width)
    hidden_four = got_hidden.reshape(groups, slots, capacity, hidden_width)
    gate_four = got_gate.reshape(groups, slots, capacity).astype(jnp.float32)[..., None]
    projected = jnp.einsum("xscd,sfd->xscf", grad_four, weights, preferred_element_type=jnp.float32)
    back_rows = (
        (gate_four * projected).astype(jnp.bfloat16).reshape(groups, block_rows, hidden_width)
    )
    back_gate = (
        jnp.sum(hidden_four.astype(jnp.float32) * projected, axis=-1)
        .astype(jnp.bfloat16)
        .reshape(groups, block_rows)
    )
    back_block = jnp.pad(back_gate[..., None], ((0, 0), (0, 0), (0, lane - 1)))
    came = lax.all_to_all(
        jnp.concatenate([back_rows, back_block], axis=-1),
        "expert",
        split_axis=0,
        concat_axis=0,
        tiled=True,
    )
    came_rows = came[..., :hidden_width]
    came_gate = came[..., hidden_width]
    d_hidden = came_rows.reshape(length, hidden_width)[places].reshape(
        tok_rows, chosen_count, hidden_width
    )
    d_gate = came_gate.reshape(length)[places].reshape(tok_rows, chosen_count)
    scaled = (gate_four * hidden_four.astype(jnp.float32)).astype(jnp.bfloat16)
    partial_value = jnp.einsum(
        "xscf,xscd->sfd", scaled, grad_four, preferred_element_type=jnp.float32
    )
    group_sum = lax.psum_scatter(partial_value, "dp", scatter_dimension=1, tiled=True)
    own_slots = lax.dynamic_slice_in_dim(flat_slots, own_index * slots, slots)
    expert_ids = jnp.arange(EXPERTS, dtype=jnp.int32)
    copies = jnp.sum((flat_slots[:, None] == expert_ids[None, :]).astype(jnp.int32), axis=0)
    is_hot = copies >= 2
    hot_rank = jnp.cumsum(is_hot.astype(jnp.int32)) - 1
    picks = own_slots[:, None] == expert_ids[None, :]
    slot_hot = jnp.any(picks & is_hot[None, :], axis=1)
    slot_rank = jnp.sum(jnp.where(picks, hot_rank[None, :], 0), axis=1)
    member = (slot_rank[:, None] == jnp.arange(HOT, dtype=jnp.int32)[None, :]) & slot_hot[:, None]
    expert_count = lax.axis_size("expert")
    halves = expert_count // HOT
    chunk_rows = 8
    chunked = group_sum.reshape(slots, halves, chunk_rows, -1)
    hot_table = jnp.sum(
        jnp.where(member[:, :, None, None, None], chunked[:, None], 0.0), axis=0
    ).reshape(expert_count, chunk_rows, -1)
    hot_total = exchange_sum(hot_table, "expert", expert_count).reshape(
        HOT, halves, chunk_rows, -1
    )
    from_table = hot_total[jnp.clip(slot_rank, 0, HOT - 1)].reshape(group_sum.shape)
    d_weight = jnp.where(slot_hot[:, None, None], from_table, group_sum)[None]
    return (d_hidden, d_gate, d_weight)


def solution(mesh):
    placed = (
        P(("dp", "expert"), None),
        P(("dp", "expert"), None, None),
        P(("dp", "expert"), None),
        P(("dp", "expert"), None),
        P(("dp", "expert"), None),
        P(),
        P("expert", None, None, None),
    )
    return jax.shard_map(
        per_device,
        mesh=mesh,
        in_specs=placed,
        out_specs=(
            P(("dp", "expert"), None, None),
            P(("dp", "expert"), None),
            P("expert", None, "dp", None),
        ),
        check_vma=False,
    )
```
